32 devices in a mesh: groups: 2 (over y), ctx: 4 (over z), head: 4 (over x, core).
Axes of the slice: x: 2, y: 2, z: 4, core: 2. Of those that a mesh axis runs over, the one named last changes fastest.
Arguments:
- hidden_in: bfloat16 [2048, 4096], P(('groups', 'ctx'), 'head'), parts along dimension 0, may hold values from -6 to 6
- norm_gain: bfloat16 [4096], P('head'), may hold values from 0.099609375 to 1.8984375
- w_query: bfloat16 [4096, 2048], P('ctx', 'head'), may hold values from -8 to 8
- w_key: bfloat16 [4096, 512], P('ctx', 'head'), may hold values from -8 to 8
- w_value: bfloat16 [4096, 512], P('ctx', 'head'), may hold values from -0.09375 to 0.09375
- w_out: bfloat16 [2048, 4096], P('head', 'ctx'), may hold values from -3 to 3
- session_ids: int32 [2048], P('groups'), parts along dimension 0, may hold values from 0 to 3, never falling along the last dimension, each value on 1 to 512 neighbouring positions
- block_anchor: int32 [16], P('groups'), parts along dimension 0, may hold values from 0 to 7, each once
Outputs:
- block_update: bfloat16 [2048, 4096], P(('groups', 'ctx'), 'head'), parts along dimension 0
The draws below stay inside these ranges and needn't reach their ends.
There are 2 independent parts, one for each index of `groups`. The reference program is written for one: setup_inputs(seed, part) draws one part's arguments, and reference() takes and returns one part's arrays. A program takes and returns all parts, laid end to end along the dimension named above; an argument that names none is the same for every part. Nothing has to cross between parts.
Inputs may be any that keep to these rules, and one draw needn't show every extreme that they name: `session_ids`: session numbers never fall along the contiguous order; 4 sessions, each of 1 to 512 tokens, one of exactly 512. `block_anchor`: each of the 8 blocks appears once.
All inputs are finite; a program needn't handle non-finite values.
Results may differ from the reference program's by a relative error of at most 0.0095.
The reference program's roundings to bfloat16 on the way count: a program that leaves them out, or rounds other values in their place, can miss the bound.
Values may be sent and summed in bfloat16 or wider, within the bound.
No kernel may reach another device: no remote copies, remote signals or barrier semaphores. Data moves between devices by JAX's collectives and lax.ppermute only.
A program may use at most 64 MiB of HBM per device.

```python
import math
import jax
import jax.numpy as jnp
import numpy as np
from jax import lax

D = 4096
HD = 128
KVH = 4
GROUP = 4
HQ = 16
BLOCK = 128
SESSIONS = 4
TOKENS = 1024
NBLK = 8
MOST = 512
N_HEAD = 4


def paired_weights(key):
    base_key = jax.random.fold_in(key, 7013)
    first_key, second_key = jax.random.split(base_key, 2)
    spread = D ** (-0.5)
    query_weight = jax.random.truncated_normal(first_key, -6.0, 6.0, (D, HQ * HD), jnp.float32) * spread
    key_weight = jax.random.truncated_normal(second_key, -6.0, 6.0, (D, KVH * HD), jnp.float32) * spread
    return (query_weight, key_weight)


def draw_w_query(key, part):
    return paired_weights(key)[0].astype(jnp.bfloat16)


def draw_w_key(key, part):
    return paired_weights(key)[1].astype(jnp.bfloat16)


def shard_levels(stream_key, dims, pieces, least, high):
    factor_of = 1.0
    for dim, parts in pieces:
        steps = jax.random.uniform(jax.random.fold_in(jax.random.fold_in(stream_key, 6), dim), (parts,), jnp.float32, least / len(pieces), high / len(pieces))
        factor_of = factor_of * jnp.repeat(jnp.exp(steps), dims[dim] // parts).reshape((-1,) + (1,) * (len(dims) - 1 - dim))
    return factor_of


def length_profile(count, total, most, skew):
    portions = [(1 << 20) // math.isqrt(standing ** skew) + 1 for standing in range(2, count + 1)]
    rest, holding = total - most - (count - 1), [1] * (count - 1)
    while rest > 0:
        candidates = [i for i in range(count - 1) if holding[i] < most]
        pool, left = sum([portions[i] for i in candidates]), rest
        for i in candidates:
            more = min(most - holding[i], max(1, left * portions[i] // pool), rest)
            holding[i] = holding[i] + more
            rest = rest - more
    return np.array([most] + holding)


def ragged(key, amount, total, bound, skew):
    if amount == 2:
        one = jax.random.randint(key, (), max(1, total - bound), min(bound, total - 1) + 1)
        return jnp.stack([one, total - one])
    tallies = jnp.asarray(length_profile(amount, total, bound, skew), jnp.int32)
    couples = (amount - 1) // 2
    giver, taker = tallies[1:1 + 2 * couples:2], tallies[2:2 + 2 * couples:2]
    margin = jnp.minimum(giver - 1, bound - taker)
    passed = jax.random.randint(jax.random.fold_in(key, 1), (couples,), 0, 1 << 20) % (margin + 1)
    tallies = tallies.at[1:1 + 2 * couples:2].set(giver - passed).at[2:2 + 2 * couples:2].set(taker + passed)
    return tallies[jax.random.permutation(jax.random.fold_in(key, 2), amount)]


def gaussian(own_key, extent, scale, bound, cuts=(), kind=jnp.bfloat16):
    array = scale * jax.random.normal(own_key, extent, jnp.float32)
    if cuts:
        array = array * shard_levels(own_key, extent, cuts, -0.22, 0.18)
    return jnp.clip(array, -bound, bound).astype(kind)


def setup_inputs(seed: int = 0, part: int = 0) -> dict:
    arg_keys = jax.random.split(jax.random.key(seed), 9)
    part_keys = jax.random.split(jax.random.fold_in(arg_keys[8], part), 9)
    return {
        "hidden_in": gaussian(part_keys[0], (TOKENS, D), 1.0, 6.0, ((0, 4), (1, 4))),
        "norm_gain": jnp.clip(1.0 + 0.18 * jax.random.normal(arg_keys[1], (D,), jnp.float32), 0.099609375, 1.8984375).astype(jnp.bfloat16),
        "w_query": draw_w_query(jax.random.fold_in(arg_keys[8], 71), part),
        "w_key": draw_w_key(jax.random.fold_in(arg_keys[8], 71), part),
        "w_value": gaussian(arg_keys[4], (D, KVH * HD), D ** -0.5, 0.09375, ((0, 4), (1, 4))),
        "w_out": gaussian(arg_keys[5], (HQ * HD, D), 0.5, 3.0, ((0, 4), (1, 4))),
        "session_ids": jnp.searchsorted(jnp.cumsum(ragged(part_keys[6], SESSIONS, TOKENS, MOST, 2)), jnp.arange(TOKENS), side="right").astype(jnp.int32),
        "block_anchor": jax.random.permutation(part_keys[7], NBLK).astype(jnp.int32),
    }


norm_epsilon = 1e-05
rotary_base = 500000.0
masked_score = -1e+30

def session_starts(session_ids):
    length = session_ids.shape[0]
    indices = jnp.arange(length, dtype=jnp.int32)
    fresh = jnp.concatenate([jnp.ones((1,), dtype=jnp.bool_), session_ids[1:] != session_ids[:-1]])
    return lax.cummax(jnp.where(fresh, indices, 0).astype(jnp.int32), axis=0)

def rotary(vectors, position):
    half_dim = vectors.shape[-1] // 2
    ladder = jnp.arange(half_dim, dtype=jnp.float32) * (2.0 / vectors.shape[-1])
    frequency = jnp.exp(-ladder * math.log(rotary_base))
    angles = position.astype(jnp.float32).reshape((-1,) + (1,) * (vectors.ndim - 1)) * frequency
    cosine = jnp.cos(angles)
    sines = jnp.sin(angles)
    first_half = vectors[..., :half_dim]
    second_half = vectors[..., half_dim:]
    return jnp.concatenate([first_half * cosine - second_half * sines, second_half * cosine + first_half * sines], axis=-1)

def reference(hidden_in, norm_gain, w_query, w_key, w_value, w_out, session_ids, block_anchor):
    tok_count = hidden_in.shape[0]
    owner_index = jnp.arange(tok_count, dtype=jnp.int32)
    contiguous = (block_anchor[owner_index // BLOCK] * BLOCK + owner_index % BLOCK).astype(jnp.int32)
    starts = session_starts(session_ids)
    session = session_ids[contiguous]
    position = contiguous - starts[contiguous]
    wide = hidden_in.astype(jnp.float32)
    normed = (wide * lax.rsqrt(lax.optimization_barrier(jnp.mean(wide * wide, axis=-1, keepdims=True)) + norm_epsilon) * norm_gain.astype(jnp.float32)).astype(jnp.bfloat16)
    query_raw = jnp.dot(normed, w_query, preferred_element_type=jnp.float32).reshape(tok_count, HQ, HD)
    key_raw = jnp.dot(normed, w_key, preferred_element_type=jnp.float32).reshape(tok_count, KVH, HD)
    values = jnp.dot(normed, w_value, preferred_element_type=jnp.float32).astype(jnp.bfloat16).reshape(tok_count, KVH, HD)
    query_heads = rotary(query_raw, position).astype(jnp.bfloat16)
    key_heads = rotary(key_raw, position).astype(jnp.bfloat16)
    allowed = (session[:, None] == session[None, :]) & (contiguous[None, :] <= contiguous[:, None])
    scale = 1.0 / math.sqrt(HD)

    def one_head(head_index):
        query_one = lax.dynamic_index_in_dim(query_heads, head_index, 1, keepdims=False)
        key_one = lax.dynamic_index_in_dim(key_heads, head_index // GROUP, 1, keepdims=False)
        value_one = lax.dynamic_index_in_dim(values, head_index // GROUP, 1, keepdims=False)
        scores = jnp.dot(query_one, key_one.T, preferred_element_type=jnp.float32) * scale
        row_max = lax.optimization_barrier(jnp.max(jnp.where(allowed, scores, masked_score), axis=1, keepdims=True))
        weights = jnp.where(allowed, jnp.exp(scores - row_max), 0.0)
        row_sum = lax.optimization_barrier(jnp.sum(weights, axis=1, keepdims=True))
        mixed = jnp.dot(weights.astype(jnp.bfloat16), value_one, preferred_element_type=jnp.float32) / row_sum
        return mixed.astype(jnp.bfloat16)
    heads = lax.map(one_head, jnp.arange(HQ, dtype=jnp.int32))
    attended = jnp.transpose(heads, (1, 0, 2)).reshape(tok_count, HQ * HD)
    group_cols = HQ * HD // N_HEAD
    total = jnp.zeros((tok_count, w_out.shape[1]), jnp.float32)
    for group_index in range(N_HEAD):
        part_cols = attended[:, group_index * group_cols:(group_index + 1) * group_cols]
        part_rows = w_out[group_index * group_cols:(group_index + 1) * group_cols, :]
        partial_sum = jnp.dot(part_cols, part_rows, preferred_element_type=jnp.float32).astype(jnp.bfloat16)
        total = total + partial_sum.astype(jnp.float32)
    return total.astype(jnp.bfloat16)
```

```python
import math

import jax
import jax.numpy as jnp
from jax import lax
from jax.sharding import PartitionSpec as P

HD = 128
GROUP = 4
BLOCK = 128


norm_epsilon = 1e-05
rotary_base = 500000.0
masked_score = -1e30


def passed_along(block, axis, distance):
    devices = range(lax.axis_size(axis))
    route = [((i - distance) % len(devices), i) for i in devices]
    return lax.ppermute(block, axis, route)


def session_starts(session_ids):
    length = session_ids.shape[0]
    indices = jnp.arange(length, dtype=jnp.int32)
    fresh = jnp.concatenate([jnp.ones((1,), dtype=jnp.bool_), session_ids[1:] != session_ids[:-1]])
    return lax.cummax(jnp.where(fresh, indices, 0), axis=0)


def rotary(vectors, position):
    half_dim = vectors.shape[-1] // 2
    ladder = jnp.arange(half_dim, dtype=jnp.float32) * (2.0 / vectors.shape[-1])
    frequency = jnp.exp(-ladder * math.log(rotary_base))
    angles = position.astype(jnp.float32).reshape((-1,) + (1,) * (vectors.ndim - 1)) * frequency
    cosine = jnp.cos(angles)
    sines = jnp.sin(angles)
    first_half = vectors[..., :half_dim]
    second_half = vectors[..., half_dim:]
    return jnp.concatenate(
        [first_half * cosine - second_half * sines, second_half * cosine + first_half * sines],
        axis=-1,
    )


def attend_core(
    carry_state, query_heads, query_pos, query_seg, key_heads, value_heads, key_pos, key_seg
):
    row_max, row_sum, mixed_sum = carry_state
    scores = jnp.einsum(
        "qagd,kad->qagk", query_heads, key_heads, preferred_element_type=jnp.float32
    ) * (1.0 / math.sqrt(query_heads.shape[-1]))
    allowed = ((query_seg[:, None] == key_seg[None, :]) & (key_pos[None, :] <= query_pos[:, None]))[
        :, None, None, :
    ]
    new_max = jnp.maximum(row_max, jnp.max(jnp.where(allowed, scores, masked_score), axis=-1))
    weights = jnp.where(allowed, jnp.exp(scores - new_max[..., None]), 0.0)
    rescale = jnp.exp(row_max - new_max)
    row_sum = row_sum * rescale + jnp.sum(weights, axis=-1)
    mixed_sum = mixed_sum * rescale[..., None] + jnp.einsum(
        "qagk,kad->qagd",
        weights.astype(jnp.bfloat16),
        value_heads,
        preferred_element_type=jnp.float32,
    )
    return (new_max, row_sum, mixed_sum)


def per_device_ring(hidden_in, norm_gain, w_query, w_key, w_value, w_out, session_ids, block_anchor):
    whole, gain_full = (
        lax.all_gather(hidden_in, "head", axis=1, tiled=True),
        lax.all_gather(norm_gain, "head", axis=0, tiled=True),
    )
    tok_rows = whole.shape[0]
    cycle_size = lax.axis_size("ctx")
    cycle_index = lax.axis_index("ctx")
    per_shard = tok_rows // BLOCK
    starts = session_starts(session_ids)
    seg_table = session_ids.reshape(-1, BLOCK)
    start_table = starts.reshape(-1, BLOCK)
    offsets = jnp.arange(BLOCK, dtype=jnp.int32)

    def token_info(owner):
        blocks_here = lax.dynamic_slice_in_dim(block_anchor, owner * per_shard, per_shard)
        contiguous = (blocks_here[:, None] * BLOCK + offsets[None, :]).reshape(-1)
        session = jnp.take(seg_table, blocks_here, axis=0).reshape(-1)
        position = contiguous - jnp.take(start_table, blocks_here, axis=0).reshape(-1)
        return (contiguous, session, position)

    wide = whole.astype(jnp.float32)
    normed = (
        wide
        * lax.rsqrt(jnp.mean(wide * wide, axis=-1, keepdims=True) + norm_epsilon)
        * gain_full.astype(jnp.float32)
    ).astype(jnp.bfloat16)
    key_cols = w_key.shape[1]
    kv_local = key_cols // HD
    pieces = (
        lax.all_gather(w_query, "ctx", axis=0, tiled=True),
        lax.all_gather(w_key, "ctx", axis=0, tiled=True),
        lax.all_gather(w_value, "ctx", axis=0, tiled=True),
    )
    query_raw, key_raw, value_raw = tuple(
        (jnp.dot(normed, weight_rows, preferred_element_type=jnp.float32) for weight_rows in pieces)
    )
    my_pos, my_seg, my_place = token_info(cycle_index)
    query_heads = rotary(query_raw.reshape(tok_rows, kv_local, GROUP, HD), my_place).astype(
        jnp.bfloat16
    )
    key_heads = rotary(key_raw.reshape(tok_rows, kv_local, HD), my_place).astype(jnp.bfloat16)
    value_heads = value_raw.astype(jnp.bfloat16).reshape(tok_rows, kv_local, HD)

    def attend(current_state, kv_stack, source):
        key_pos, key_seg, unused_place = token_info(source)
        return attend_core(
            current_state, query_heads, my_pos, my_seg, kv_stack[0], kv_stack[1], key_pos, key_seg
        )

    carry_state = (
        jnp.full((tok_rows, kv_local, GROUP), masked_score, jnp.float32),
        jnp.zeros((tok_rows, kv_local, GROUP), jnp.float32),
        jnp.zeros((tok_rows, kv_local, GROUP, HD), jnp.float32),
    )
    own_stack = jnp.stack([key_heads, value_heads])
    carry_state = attend(carry_state, own_stack, cycle_index)

    def cycle_turn(turn_index, loop_carry):
        current_state, moving = loop_carry
        moving = passed_along(moving, "ctx", 1)
        current_state = attend(current_state, moving, (cycle_index - turn_index) % cycle_size)
        return (current_state, moving)

    carry_state, unused_stack = lax.fori_loop(1, cycle_size, cycle_turn, (carry_state, own_stack))
    final_max, row_sum, mixed_sum = carry_state
    attended = (mixed_sum / row_sum[..., None]).astype(jnp.bfloat16).reshape(tok_rows, -1)
    terms = jnp.dot(
        attended,
        lax.all_gather(w_out, "ctx", axis=1, tiled=True),
        preferred_element_type=jnp.float32,
    )
    return lax.psum_scatter(terms.astype(jnp.bfloat16), "head", scatter_dimension=1, tiled=True)


def token_table(session_ids, block_anchor, owners_rows):
    starts = session_starts(session_ids)
    owner = jnp.arange(owners_rows, dtype=jnp.int32)
    contiguous = jnp.take(block_anchor, owner // BLOCK) * BLOCK + owner % BLOCK
    session = jnp.take(session_ids, contiguous)
    position = contiguous - jnp.take(starts, contiguous)
    return contiguous, session, position


def transposed(block, n):
    route = [(c * n + h, h * n + c) for c in range(n) for h in range(n)]
    return lax.ppermute(block, ("ctx", "head"), route)


def per_device_ws(hidden_in, norm_gain, w_query, w_key, w_value, w_out, session_ids, block_anchor):
    n = lax.axis_size("ctx")
    cycle_index = lax.axis_index("ctx")
    tok_rows, local_feats = hidden_in.shape
    wide = hidden_in.astype(jnp.float32)
    squares = lax.psum(jnp.sum(wide * wide, axis=-1, keepdims=True), "head")
    normed = (
        wide
        * lax.rsqrt(squares / (local_feats * n) + norm_epsilon)
        * norm_gain.astype(jnp.float32)
    ).astype(jnp.bfloat16)
    every = lax.all_gather(transposed(normed, n), "head", axis=0, tiled=True)
    q_cols, k_cols = w_query.shape[1], w_key.shape[1]
    stacked = jnp.concatenate([w_query, w_key, w_value], axis=1)
    partial = jnp.dot(every, stacked, preferred_element_type=jnp.float32)
    mine = lax.psum_scatter(partial, "ctx", scatter_dimension=0, tiled=True)
    kv_local = k_cols // HD
    query_raw = mine[:, :q_cols].reshape(tok_rows, kv_local, GROUP, HD)
    key_raw = mine[:, q_cols : q_cols + k_cols].reshape(tok_rows, kv_local, HD)
    value_raw = mine[:, q_cols + k_cols :].reshape(tok_rows, kv_local, HD)
    contiguous, session, position = token_table(session_ids, block_anchor, tok_rows * n)
    my_pos = lax.dynamic_slice_in_dim(contiguous, cycle_index * tok_rows, tok_rows)
    my_seg = lax.dynamic_slice_in_dim(session, cycle_index * tok_rows, tok_rows)
    my_place = lax.dynamic_slice_in_dim(position, cycle_index * tok_rows, tok_rows)
    query_heads = rotary(query_raw, my_place).astype(jnp.bfloat16)
    key_heads = rotary(key_raw, my_place).astype(jnp.bfloat16)
    value_heads = value_raw.astype(jnp.bfloat16)
    kv_all = lax.all_gather(jnp.stack([key_heads, value_heads]), "ctx", axis=1, tiled=True)
    scores = jnp.einsum(
        "qagd,kad->qagk", query_heads, kv_all[0], preferred_element_type=jnp.float32
    ) * (1.0 / math.sqrt(HD))
    allowed = ((my_seg[:, None] == session[None, :]) & (contiguous[None, :] <= my_pos[:, None]))[
        :, None, None, :
    ]
    row_max = jnp.max(jnp.where(allowed, scores, masked_score), axis=-1, keepdims=True)
    weights = jnp.where(allowed, jnp.exp(scores - row_max), 0.0)
    row_sum = jnp.sum(weights, axis=-1, keepdims=True)
    mixed = jnp.einsum(
        "qagk,kad->qagd", weights.astype(jnp.bfloat16), kv_all[1], preferred_element_type=jnp.float32
    )
    attended = (mixed / row_sum).astype(jnp.bfloat16).reshape(tok_rows, -1)
    att_all = lax.all_gather(attended, "ctx", axis=0, tiled=True)
    terms = jnp.dot(att_all, w_out, preferred_element_type=jnp.float32).astype(jnp.bfloat16)
    summed = lax.psum_scatter(terms, "head", scatter_dimension=0, tiled=True)
    return transposed(summed, n)


def solution(mesh):
    in_specs = (
        P(("groups", "ctx"), "head"),
        P("head"),
        P("ctx", "head"),
        P("ctx", "head"),
        P("ctx", "head"),
        P("head", "ctx"),
        P("groups"),
        P("groups"),
    )
    out_specs = P(("groups", "ctx"), "head")
    square = mesh.shape["ctx"] == mesh.shape["head"]
    per_device = per_device_ws if square else per_device_ring
    return jax.shard_map(
        per_device, mesh=mesh, in_specs=in_specs, out_specs=out_specs, check_vma=False
    )
```

```python
import math

import jax
import jax.numpy as jnp
from jax import lax
from jax.sharding import PartitionSpec as P

HD = 128
GROUP = 4
BLOCK = 128


norm_epsilon = 1e-05
rotary_base = 500000.0
masked_score = -1e30


def passed_along(block, axis, distance):
    devices = range(lax.axis_size(axis))
    route = [((i - distance) % len(devices), i) for i in devices]
    return lax.ppermute(block, axis, route)


def session_starts(session_ids):
    length = session_ids.shape[0]
    indices = jnp.arange(length, dtype=jnp.int32)
    fresh = jnp.concatenate([jnp.ones((1,), dtype=jnp.bool_), session_ids[1:] != session_ids[:-1]])
    return lax.cummax(jnp.where(fresh, indices, 0), axis=0)


def rotary(vectors, position):
    half_dim = vectors.shape[-1] // 2
    ladder = jnp.arange(half_dim, dtype=jnp.float32) * (2.0 / vectors.shape[-1])
    frequency = jnp.exp(-ladder * math.log(rotary_base))
    angles = position.astype(jnp.float32).reshape((-1,) + (1,) * (vectors.ndim - 1)) * frequency
    cosine = jnp.cos(angles)
    sines = jnp.sin(angles)
    first_half = vectors[..., :half_dim]
    second_half = vectors[..., half_dim:]
    return jnp.concatenate(
        [first_half * cosine - second_half * sines, second_half * cosine + first_half * sines],
        axis=-1,
    )


def attend_core(
    carry_state, query_heads, query_pos, query_seg, key_heads, value_heads, key_pos, key_seg
):
    row_max, row_sum, mixed_sum = carry_state
    scores = jnp.einsum(
        "qagd,kad->qagk", query_heads, key_heads, preferred_element_type=jnp.float32
    ) * (1.0 / math.sqrt(query_heads.shape[-1]))
    allowed = ((query_seg[:, None] == key_seg[None, :]) & (key_pos[None, :] <= query_pos[:, None]))[
        :, None, None, :
    ]
    new_max = jnp.maximum(row_max, jnp.max(jnp.where(allowed, scores, masked_score), axis=-1))
    weights = jnp.where(allowed, jnp.exp(scores - new_max[..., None]), 0.0)
    rescale = jnp.exp(row_max - new_max)
    row_sum = row_sum * rescale + jnp.sum(weights, axis=-1)
    mixed_sum = mixed_sum * rescale[..., None] + jnp.einsum(
        "qagk,kad->qagd",
        weights.astype(jnp.bfloat16),
        value_heads,
        preferred_element_type=jnp.float32,
    )
    return (new_max, row_sum, mixed_sum)


def per_device_ring(hidden_in, norm_gain, w_query, w_key, w_value, w_out, session_ids, block_anchor):
    whole, gain_full = (
        lax.all_gather(hidden_in, "head", axis=1, tiled=True),
        lax.all_gather(norm_gain, "head", axis=0, tiled=True),
    )
    tok_rows = whole.shape[0]
    cycle_size = lax.axis_size("ctx")
    cycle_index = lax.axis_index("ctx")
    per_shard = tok_rows // BLOCK
    starts = session_starts(session_ids)
    seg_table = session_ids.reshape(-1, BLOCK)
    start_table = starts.reshape(-1, BLOCK)
    offsets = jnp.arange(BLOCK, dtype=jnp.int32)

    def token_info(owner):
        blocks_here = lax.dynamic_slice_in_dim(block_anchor, owner * per_shard, per_shard)
        contiguous = (blocks_here[:, None] * BLOCK + offsets[None, :]).reshape(-1)
        session = jnp.take(seg_table, blocks_here, axis=0).reshape(-1)
        position = contiguous - jnp.take(start_table, blocks_here, axis=0).reshape(-1)
        return (contiguous, session, position)

    wide = whole.astype(jnp.float32)
    normed = (
        wide
        * lax.rsqrt(jnp.mean(wide * wide, axis=-1, keepdims=True) + norm_epsilon)
        * gain_full.astype(jnp.float32)
    ).astype(jnp.bfloat16)
    key_cols = w_key.shape[1]
    kv_local = key_cols // HD
    pieces = (
        lax.all_gather(w_query, "ctx", axis=0, tiled=True),
        lax.all_gather(w_key, "ctx", axis=0, tiled=True),
        lax.all_gather(w_value, "ctx", axis=0, tiled=True),
    )
    query_raw, key_raw, value_raw = tuple(
        (jnp.dot(normed, weight_rows, preferred_element_type=jnp.float32) for weight_rows in pieces)
    )
    my_pos, my_seg, my_place = token_info(cycle_index)
    query_heads = rotary(query_raw.reshape(tok_rows, kv_local, GROUP, HD), my_place).astype(
        jnp.bfloat16
    )
    key_heads = rotary(key_raw.reshape(tok_rows, kv_local, HD), my_place).astype(jnp.bfloat16)
    value_heads = value_raw.astype(jnp.bfloat16).reshape(tok_rows, kv_local, HD)

    def attend(current_state, kv_stack, source):
        key_pos, key_seg, unused_place = token_info(source)
        return attend_core(
            current_state, query_heads, my_pos, my_seg, kv_stack[0], kv_stack[1], key_pos, key_seg
        )

    carry_state = (
        jnp.full((tok_rows, kv_local, GROUP), masked_score, jnp.float32),
        jnp.zeros((tok_rows, kv_local, GROUP), jnp.float32),
        jnp.zeros((tok_rows, kv_local, GROUP, HD), jnp.float32),
    )
    own_stack = jnp.stack([key_heads, value_heads])
    carry_state = attend(carry_state, own_stack, cycle_index)

    def cycle_turn(turn_index, loop_carry):
        current_state, moving = loop_carry
        moving = passed_along(moving, "ctx", 1)
        current_state = attend(current_state, moving, (cycle_index - turn_index) % cycle_size)
        return (current_state, moving)

    carry_state, unused_stack = lax.fori_loop(1, cycle_size, cycle_turn, (carry_state, own_stack))
    final_max, row_sum, mixed_sum = carry_state
    attended = (mixed_sum / row_sum[..., None]).astype(jnp.bfloat16).reshape(tok_rows, -1)
    terms = jnp.dot(
        attended,
        lax.all_gather(w_out, "ctx", axis=1, tiled=True),
        preferred_element_type=jnp.float32,
    )
    return lax.psum_scatter(terms.astype(jnp.bfloat16), "head", scatter_dimension=1, tiled=True)


def token_table(session_ids, block_anchor):
    offsets = jnp.arange(BLOCK, dtype=jnp.int32)
    contiguous = (block_anchor[:, None] * BLOCK + offsets[None, :]).reshape(-1)
    seg_table = session_ids.reshape(-1, BLOCK)
    start_table = session_starts(session_ids).reshape(-1, BLOCK)
    session = jnp.take(seg_table, block_anchor, axis=0).reshape(-1)
    position = contiguous - jnp.take(start_table, block_anchor, axis=0).reshape(-1)
    return contiguous, session, position


def transposed(block, n):
    route = [(c * n + h, h * n + c) for c in range(n) for h in range(n)]
    return lax.ppermute(block, ("ctx", "head"), route)


def line_gather(block, axis, n):
    me = lax.axis_index(axis)
    parts = [block] + [passed_along(block, axis, d) for d in range(1, n)]
    stacked = jnp.stack(parts)
    source_slot = (me - jnp.arange(n, dtype=jnp.int32)) % n
    return jnp.take(stacked, source_slot, axis=0).reshape((-1,) + block.shape[1:])


def xor_swap(block, axis, n, d):
    return lax.ppermute(block, axis, [(i, i ^ d) for i in range(n)])


def halving_gather(block, axis, n):
    me = lax.axis_index(axis)
    offsets = [0]
    held = block[None]
    d = n // 2
    while d >= 1:
        held = jnp.concatenate([held, xor_swap(held, axis, n, d)])
        offsets = offsets + [o ^ d for o in offsets]
        d //= 2
    slot_of = jnp.asarray([offsets.index(o) for o in range(n)], jnp.int32)
    order = jnp.take(slot_of, me ^ jnp.arange(n, dtype=jnp.int32))
    return jnp.take(held, order, axis=0).reshape((-1,) + block.shape[1:])


def halving_scatter(block, axis, n):
    me = lax.axis_index(axis)
    rows = block.shape[0] // n
    held = block.reshape((n, rows) + block.shape[1:])
    total = None
    d = 1
    while d < n:
        count = held.shape[0]
        slots = jnp.arange(count // 2, dtype=jnp.int32)
        mine_bit = (me // d) % 2
        keep = jnp.take(held, slots * 2 + mine_bit, axis=0)
        send = jnp.take(held, slots * 2 + 1 - mine_bit, axis=0)
        if total is not None:
            keep_sum = jnp.take(total, slots * 2 + mine_bit, axis=0)
            send_sum = jnp.take(total, slots * 2 + 1 - mine_bit, axis=0)
            keep = keep_sum
            send = send_sum.astype(block.dtype)
        total = keep.astype(jnp.float32) + xor_swap(send, axis, n, d).astype(jnp.float32)
        held = total
        d *= 2
    return total[0].astype(block.dtype)


def per_device_ws(hidden_in, norm_gain, w_query, w_key, w_value, w_out, session_ids, block_anchor):
    n = lax.axis_size("ctx")
    cycle_index = lax.axis_index("ctx")
    tok_rows, local_feats = hidden_in.shape
    moved = transposed(hidden_in, n)
    wide = hidden_in.astype(jnp.float32)
    squares = lax.psum(jnp.sum(wide * wide, axis=-1), "head")
    scale_rows = lax.rsqrt(squares / (local_feats * n) + norm_epsilon)
    side = transposed(jnp.concatenate([scale_rows, norm_gain.astype(jnp.float32)]), n)
    normed = (
        moved.astype(jnp.float32) * side[:tok_rows, None] * side[None, tok_rows:]
    ).astype(jnp.bfloat16)
    every = halving_gather(normed, "head", n)
    q_cols, k_cols = w_query.shape[1], w_key.shape[1]
    kv_local = k_cols // HD
    part_kv = jnp.dot(
        every, jnp.concatenate([w_key, w_value], axis=1), preferred_element_type=jnp.float32
    )
    part_q = jnp.dot(every, w_query, preferred_element_type=jnp.float32)
    mine_kv = lax.psum_scatter(part_kv, "ctx", scatter_dimension=0, tiled=True)
    mine_q = lax.psum_scatter(part_q, "ctx", scatter_dimension=0, tiled=True)
    contiguous, session, position = token_table(session_ids, block_anchor)
    my_pos = lax.dynamic_slice_in_dim(contiguous, cycle_index * tok_rows, tok_rows)
    my_seg = lax.dynamic_slice_in_dim(session, cycle_index * tok_rows, tok_rows)
    my_place = lax.dynamic_slice_in_dim(position, cycle_index * tok_rows, tok_rows)
    key_heads = rotary(mine_kv[:, :k_cols].reshape(tok_rows, kv_local, HD), my_place)
    kv_rows = jnp.concatenate(
        [key_heads.astype(jnp.bfloat16).reshape(tok_rows, k_cols), mine_kv[:, k_cols:].astype(jnp.bfloat16)],
        axis=1,
    )
    kv_all = line_gather(kv_rows, "ctx", n)
    keys = kv_all[:, :k_cols].reshape(-1, kv_local, HD)
    values = kv_all[:, k_cols:].reshape(-1, kv_local, HD)
    query_heads = rotary(mine_q.reshape(tok_rows, kv_local, GROUP, HD), my_place).astype(jnp.bfloat16)
    scores = jnp.einsum(
        "qagd,kad->qagk", query_heads, keys, preferred_element_type=jnp.float32
    ) * (1.0 / math.sqrt(HD))
    allowed = ((my_seg[:, None] == session[None, :]) & (contiguous[None, :] <= my_pos[:, None]))[
        :, None, None, :
    ]
    row_max = jnp.max(jnp.where(allowed, scores, masked_score), axis=-1, keepdims=True)
    weights = jnp.where(allowed, jnp.exp(scores - row_max), 0.0)
    row_sum = jnp.sum(weights, axis=-1, keepdims=True)
    mixed = jnp.einsum(
        "qagk,kad->qagd", weights.astype(jnp.bfloat16), values, preferred_element_type=jnp.float32
    )
    attended = (mixed / row_sum).astype(jnp.bfloat16).reshape(tok_rows, -1)
    att_all = line_gather(attended, "ctx", n)
    terms = jnp.dot(att_all, w_out, preferred_element_type=jnp.float32).astype(jnp.bfloat16)
    summed = halving_scatter(terms, "head", n)
    return transposed(summed, n)


def solution(mesh):
    in_specs = (
        P(("groups", "ctx"), "head"),
        P("head"),
        P("ctx", "head"),
        P("ctx", "head"),
        P("ctx", "head"),
        P("head", "ctx"),
        P("groups"),
        P("groups"),
    )
    out_specs = P(("groups", "ctx"), "head")
    n_head = mesh.shape["head"]
    square = mesh.shape["ctx"] == n_head and n_head & (n_head - 1) == 0
    per_device = per_device_ws if square else per_device_ring
    return jax.shard_map(
        per_device, mesh=mesh, in_specs=in_specs, out_specs=out_specs, check_vma=False
    )
```
